32 devices in a mesh: depth: 4 (over y, x), lat: 8 (over z, core).
Axes of the slice: x: 2, y: 2, z: 4, core: 2. Of those that a mesh axis runs over, the one named last changes fastest.
Arguments:
- sources: bfloat16 [4, 8, 32, 2048], P('depth', 'lat'), may hold values from -6 to 6
- coupling: float32 [4, 8, 2048], P('depth', 'lat'), may hold values from 0.2 to 0.6
- merge_ops: bfloat16 [4, 8, 2048, 2048], P('depth', 'lat'), may hold values from -1 to 1.5
Outputs:
- solution: bfloat16 [4, 8, 32, 2048], P('depth', 'lat')
The draws below stay inside these ranges and needn't reach their ends.
All inputs are finite; a program needn't handle non-finite values.
Results may differ from the reference program's by a relative error of at most 0.03.
Values may be sent and summed in bfloat16 or wider, within the bound.
No kernel may reach another device: no remote copies, remote signals or barrier semaphores. Data moves between devices by JAX's collectives and lax.ppermute only.
A program may use at most 64 MiB of HBM per device.

```python
import math
import jax
import jax.numpy as jnp
from jax import lax

IW = 2048
SHOTS = 32
LAYERS = 4
PATCHES = 8
LEVELS = 3


def draw_merge_ops(key, part):
    key_diag = jax.random.fold_in(key, 11)
    key_off = jax.random.fold_in(key, 12)
    full_shape = (LAYERS, PATCHES, IW, IW)
    off_part = jax.random.normal(key_off, full_shape, jnp.float32) * (0.4 / math.sqrt(IW))
    diag_part = jax.random.uniform(key_diag, (LAYERS, PATCHES, 1, IW), jnp.float32, 0.7, 1.3)
    identity = jnp.eye(IW, dtype=jnp.float32)[None, None]
    return (off_part + identity * diag_part).astype(jnp.bfloat16)


def block_levels(own_key, dims, split, low, top_value):
    factor_of = 1.0
    for dim, parts in split:
        draws = jax.random.uniform(jax.random.fold_in(jax.random.fold_in(own_key, 6), dim), (parts,), jnp.float32, low / len(split), top_value / len(split))
        factor_of = factor_of * jnp.repeat(jnp.exp(draws), dims[dim] // parts).reshape((-1,) + (1,) * (len(dims) - 1 - dim))
    return factor_of


def scatter_about(key, shape, scale, reach, split=(), kind=jnp.bfloat16):
    drawn = scale * jax.random.normal(key, shape, jnp.float32)
    if split:
        drawn = drawn * block_levels(key, shape, split, -0.22, 0.18)
    return jnp.clip(drawn, -reach, reach).astype(kind)


def setup_inputs(seed: int = 0) -> dict:
    keys = jax.random.split(jax.random.key(seed), 4)
    return {
        "sources": scatter_about(keys[0], (LAYERS, PATCHES, SHOTS, IW), 1.0, 6.0, ((0, 4), (1, 8))),
        "coupling": jnp.clip(jnp.exp(math.log(0.6) - 1.0986123 * jax.random.uniform(keys[1], (LAYERS, PATCHES, IW), jnp.float32) ** block_levels(keys[1], (LAYERS, PATCHES, IW), ((0, 4), (1, 8)), -0.2, 0.2)), 0.2, 0.6),
        "merge_ops": draw_merge_ops(jax.random.fold_in(keys[3], 71), 0),
    }


half_root = 0.7071067811865476


def apply_each(vectors, operators, transposed):
    def one_node(paired):
        if transposed:
            return jnp.dot(paired[0], paired[1].T, preferred_element_type=jnp.float32).astype(jnp.bfloat16)
        return jnp.dot(paired[0], paired[1], preferred_element_type=jnp.float32).astype(jnp.bfloat16)
    return lax.map(one_node, (vectors, operators))


def haar_level(values, bit_level):
    group = 2 ** bit_level
    shaped = values.reshape((PATCHES // (2 * group), 2, group) + values.shape[1:]).astype(jnp.float32)
    lower = shaped[:, 0]
    upper = shaped[:, 1]
    mixed = jnp.stack([(lower + upper) * half_root, (lower - upper) * half_root], axis=1)
    return mixed.reshape(values.shape).astype(jnp.bfloat16)


def reference(sources, coupling, merge_ops):
    incoming = jnp.zeros(sources.shape[1:], jnp.bfloat16)
    outputs = []
    for layer_index in range(LAYERS):
        leaf_data = (sources[layer_index].astype(jnp.float32) + coupling[layer_index][:, None, :] * incoming.astype(jnp.float32)).astype(jnp.bfloat16)
        values = leaf_data
        for bit_level in range(LEVELS):
            values = apply_each(haar_level(values, bit_level), merge_ops[layer_index], False)
        values = apply_each(values, merge_ops[layer_index], True)
        for bit_level in range(LEVELS - 1, -1, -1):
            values = haar_level(values, bit_level)
        outputs.append(values)
        incoming = values
    return jnp.stack(outputs)
```

```python
import functools

import jax
import jax.numpy as jnp
from jax import lax
from jax.experimental import pallas as pl
from jax.experimental.pallas import tpu as pltpu
from jax.sharding import PartitionSpec as P

half_root = 0.7071067811865476
TILE = 512


def partner_2(block, axis, apart):
    count = lax.axis_size(axis)
    route = []
    for low in range(count):
        high = low | 1 << apart
        if high != low and high < count:
            route += [(low, high), (high, low)]
    return lax.ppermute(block, axis, route)


def shifted(array, axis, by):
    length = lax.axis_size(axis)
    pairs = [(i, i + by) for i in range(length) if 0 <= i + by < length]
    return lax.ppermute(array, axis, pairs)


def mixed_dot_kernel(sign_ref, values_ref, partner_ref, op_ref, out_ref):
    first = values_ref[...].astype(jnp.float32)
    second = partner_ref[...].astype(jnp.float32)
    mixed = ((second + sign_ref[...] * first) * half_root).astype(jnp.bfloat16)
    width = op_ref.shape[1]
    for start in range(0, width, TILE):
        out_ref[:, start:start + TILE] = jnp.dot(
            mixed, op_ref[:, start:start + TILE], preferred_element_type=jnp.float32
        ).astype(out_ref.dtype)


def transposed_dot_kernel(values_ref, op_ref, out_ref):
    values = values_ref[...]
    width = op_ref.shape[0]
    for start in range(0, width, TILE):
        out_ref[:, start:start + TILE] = lax.dot_general(
            values,
            op_ref[start:start + TILE, :],
            (((1,), (1,)), ((), ())),
            preferred_element_type=jnp.float32,
        ).astype(out_ref.dtype)


def vmem_spec():
    return pl.BlockSpec(memory_space=pltpu.VMEM)


def cost(rows, width):
    return pl.CostEstimate(
        flops=2 * rows * width * width,
        bytes_accessed=2 * width * width + 6 * rows * width,
        transcendentals=0,
    )


def mixed_dot(sign, values, partner, merge_op):
    rows, width = values.shape
    return pl.pallas_call(
        mixed_dot_kernel,
        out_shape=jax.ShapeDtypeStruct(values.shape, jnp.bfloat16),
        in_specs=[vmem_spec()] * 4,
        out_specs=vmem_spec(),
        cost_estimate=cost(rows, width),
        compiler_params=pltpu.CompilerParams(vmem_limit_bytes=4 * 1024 * 1024),
    )(sign, values, partner, pltpu.with_memory_space_constraint(merge_op, pltpu.VMEM))


def transposed_dot(values, merge_op):
    rows, width = values.shape
    return pl.pallas_call(
        transposed_dot_kernel,
        out_shape=jax.ShapeDtypeStruct(values.shape, jnp.bfloat16),
        in_specs=[vmem_spec()] * 2,
        out_specs=vmem_spec(),
        cost_estimate=cost(rows, width),
        compiler_params=pltpu.CompilerParams(vmem_limit_bytes=4 * 1024 * 1024),
    )(values, pltpu.with_memory_space_constraint(merge_op, pltpu.VMEM))


def haar_pair(values, partner, lat_index, bit_level):
    is_lower = lat_index // 2**bit_level % 2 == 0
    first = values.astype(jnp.float32)
    second = partner.astype(jnp.float32)
    return jnp.where(is_lower, (first + second) * half_root, (second - first) * half_root).astype(
        jnp.bfloat16
    )


def level_sign(lat_index, bit_level, width):
    is_lower = lat_index // 2**bit_level % 2 == 0
    return jnp.full((1, width), jnp.where(is_lower, 1.0, -1.0), jnp.float32)


def sweep_layer(leaf_data, merge_op):
    lat_count = lax.axis_size("lat")
    lat_index = lax.axis_index("lat")
    levels = lat_count.bit_length() - 1
    width = leaf_data.shape[1]
    values = leaf_data
    for bit_level in range(levels):
        partner = partner_2(values, "lat", bit_level)
        values = mixed_dot(level_sign(lat_index, bit_level, width), values, partner, merge_op)
    values = transposed_dot(values, merge_op)
    for bit_level in range(levels - 1, -1, -1):
        partner = partner_2(values, "lat", bit_level)
        values = haar_pair(values, partner, lat_index, bit_level)
    return values


def on_device(sources, coupling, merge_ops):
    merge_op = merge_ops[0, 0]
    coupling_row = coupling[0, 0]
    depth_index = lax.axis_index("depth")
    depth_count = lax.axis_size("depth")
    shot_rows = sources[0, 0]
    result = jnp.zeros_like(shot_rows)
    incoming = jnp.zeros_like(shot_rows)
    for sweep_step in range(depth_count):
        leaf_data = (
            shot_rows.astype(jnp.float32) + coupling_row * incoming.astype(jnp.float32)
        ).astype(jnp.bfloat16)
        solved = sweep_layer(leaf_data, merge_op)
        result = jnp.where(depth_index == sweep_step, solved, result)
        if sweep_step + 1 < depth_count:
            incoming = shifted(solved, "depth", 1)
    return result[None, None]


def solution(mesh):
    return jax.shard_map(
        on_device,
        mesh=mesh,
        in_specs=(
            P("depth", "lat", None, None),
            P("depth", "lat", None),
            P("depth", "lat", None, None),
        ),
        out_specs=P("depth", "lat", None, None),
        check_vma=False,
    )
```

```python
import functools

import jax
import jax.numpy as jnp
from jax import lax
from jax.experimental import pallas as pl
from jax.experimental.pallas import tpu as pltpu
from jax.sharding import PartitionSpec as P

half_root = 0.7071067811865476
TILE = 512
CHUNKS = 2


def partner_2(block, axis, apart):
    count = lax.axis_size(axis)
    route = []
    for low in range(count):
        high = low | 1 << apart
        if high != low and high < count:
            route += [(low, high), (high, low)]
    return lax.ppermute(block, axis, route)


def shifted(array, axis, by):
    length = lax.axis_size(axis)
    pairs = [(i, i + by) for i in range(length) if 0 <= i + by < length]
    return lax.ppermute(array, axis, pairs)


def mixed_dot_kernel(sign_ref, values_ref, partner_ref, op_ref, out_ref):
    first = values_ref[...].astype(jnp.float32)
    second = partner_ref[...].astype(jnp.float32)
    mixed = ((second + sign_ref[...] * first) * half_root).astype(jnp.bfloat16)
    width = op_ref.shape[1]
    for start in range(0, width, TILE):
        out_ref[:, start:start + TILE] = jnp.dot(
            mixed, op_ref[:, start:start + TILE], preferred_element_type=jnp.float32
        ).astype(out_ref.dtype)


def transposed_dot_kernel(values_ref, op_ref, out_ref):
    values = values_ref[...]
    width = op_ref.shape[0]
    for start in range(0, width, TILE):
        out_ref[:, start:start + TILE] = lax.dot_general(
            values,
            op_ref[start:start + TILE, :],
            (((1,), (1,)), ((), ())),
            preferred_element_type=jnp.float32,
        ).astype(out_ref.dtype)


def vmem_spec():
    return pl.BlockSpec(memory_space=pltpu.VMEM)


def cost(rows, width):
    return pl.CostEstimate(
        flops=2 * rows * width * width,
        bytes_accessed=2 * width * width + 6 * rows * width,
        transcendentals=0,
    )


def mixed_dot(sign, values, partner, merge_op):
    rows, width = values.shape
    return pl.pallas_call(
        mixed_dot_kernel,
        out_shape=jax.ShapeDtypeStruct(values.shape, jnp.bfloat16),
        in_specs=[vmem_spec()] * 4,
        out_specs=vmem_spec(),
        cost_estimate=cost(rows, width),
        compiler_params=pltpu.CompilerParams(vmem_limit_bytes=4 * 1024 * 1024),
    )(sign, values, partner, pltpu.with_memory_space_constraint(merge_op, pltpu.VMEM))


def transposed_dot(values, merge_op):
    rows, width = values.shape
    return pl.pallas_call(
        transposed_dot_kernel,
        out_shape=jax.ShapeDtypeStruct(values.shape, jnp.bfloat16),
        in_specs=[vmem_spec()] * 2,
        out_specs=vmem_spec(),
        cost_estimate=cost(rows, width),
        compiler_params=pltpu.CompilerParams(vmem_limit_bytes=4 * 1024 * 1024),
    )(values, pltpu.with_memory_space_constraint(merge_op, pltpu.VMEM))


def haar_pair(values, partner, lat_index, bit_level):
    is_lower = lat_index // 2**bit_level % 2 == 0
    first = values.astype(jnp.float32)
    second = partner.astype(jnp.float32)
    return jnp.where(is_lower, (first + second) * half_root, (second - first) * half_root).astype(
        jnp.bfloat16
    )


def level_sign(lat_index, bit_level, width):
    is_lower = lat_index // 2**bit_level % 2 == 0
    return jnp.full((1, width), jnp.where(is_lower, 1.0, -1.0), jnp.float32)


def sweep_layer(leaf_data, merge_op):
    lat_count = lax.axis_size("lat")
    lat_index = lax.axis_index("lat")
    levels = lat_count.bit_length() - 1
    width = leaf_data.shape[1]
    values = leaf_data
    for bit_level in range(levels):
        partner = partner_2(values, "lat", bit_level)
        values = mixed_dot(level_sign(lat_index, bit_level, width), values, partner, merge_op)
    values = transposed_dot(values, merge_op)
    for bit_level in range(levels - 1, -1, -1):
        partner = partner_2(values, "lat", bit_level)
        values = haar_pair(values, partner, lat_index, bit_level)
    return values


def on_device(sources, coupling, merge_ops):
    merge_op = merge_ops[0, 0]
    coupling_row = coupling[0, 0]
    depth_index = lax.axis_index("depth")
    depth_count = lax.axis_size("depth")
    shot_rows = sources[0, 0]
    rows = shot_rows.shape[0]
    chunks = CHUNKS
    chunk = rows // chunks
    result = jnp.zeros_like(shot_rows)
    incoming = jnp.zeros((chunk, shot_rows.shape[1]), shot_rows.dtype)
    steps = chunks + depth_count - 1
    for step in range(steps):
        position = step - depth_index
        valid = (position >= 0) & (position < chunks)
        start = jnp.clip(position, 0, chunks - 1) * chunk
        own = lax.dynamic_slice_in_dim(shot_rows, start, chunk, 0)
        leaf_data = (own.astype(jnp.float32) + coupling_row * incoming.astype(jnp.float32)).astype(
            jnp.bfloat16
        )
        solved = sweep_layer(leaf_data, merge_op)
        result = jnp.where(valid, lax.dynamic_update_slice_in_dim(result, solved, start, 0), result)
        if step + 1 < steps:
            incoming = shifted(solved, "depth", 1)
    return result[None, None]


def solution(mesh):
    return jax.shard_map(
        on_device,
        mesh=mesh,
        in_specs=(
            P("depth", "lat", None, None),
            P("depth", "lat", None),
            P("depth", "lat", None, None),
        ),
        out_specs=P("depth", "lat", None, None),
        check_vma=False,
    )
```

```python
import functools

import jax
import jax.numpy as jnp
from jax import lax
from jax.experimental import pallas as pl
from jax.experimental.pallas import tpu as pltpu
from jax.sharding import PartitionSpec as P

half_root = 0.7071067811865476
TILE = 512


def partner_2(block, axis, apart):
    count = lax.axis_size(axis)
    route = []
    for low in range(count):
        high = low | 1 << apart
        if high != low and high < count:
            route += [(low, high), (high, low)]
    return lax.ppermute(block, axis, route)


def shifted(array, axis, by):
    length = lax.axis_size(axis)
    pairs = [(i, i + by) for i in range(length) if 0 <= i + by < length]
    return lax.ppermute(array, axis, pairs)


def mixed_dot_kernel(sign_ref, values_ref, partner_ref, op_ref, out_ref):
    first = values_ref[...].astype(jnp.float32)
    second = partner_ref[...].astype(jnp.float32)
    mixed = ((second + sign_ref[...] * first) * half_root).astype(jnp.bfloat16)
    width = op_ref.shape[1]
    for start in range(0, width, TILE):
        out_ref[:, start:start + TILE] = jnp.dot(
            mixed, op_ref[:, start:start + TILE], preferred_element_type=jnp.float32
        ).astype(out_ref.dtype)


def transposed_dot_kernel(values_ref, op_ref, out_ref):
    values = values_ref[...]
    width = op_ref.shape[0]
    for start in range(0, width, TILE):
        out_ref[:, start:start + TILE] = lax.dot_general(
            values,
            op_ref[start:start + TILE, :],
            (((1,), (1,)), ((), ())),
            preferred_element_type=jnp.float32,
        ).astype(out_ref.dtype)


def vmem_spec():
    return pl.BlockSpec(memory_space=pltpu.VMEM)


def cost(rows, width):
    return pl.CostEstimate(
        flops=2 * rows * width * width,
        bytes_accessed=2 * width * width + 6 * rows * width,
        transcendentals=0,
    )


def mixed_dot(sign, values, partner, merge_op):
    rows, width = values.shape
    return pl.pallas_call(
        mixed_dot_kernel,
        out_shape=jax.ShapeDtypeStruct(values.shape, jnp.bfloat16),
        in_specs=[vmem_spec()] * 4,
        out_specs=vmem_spec(),
        cost_estimate=cost(rows, width),
        compiler_params=pltpu.CompilerParams(vmem_limit_bytes=4 * 1024 * 1024),
    )(sign, values, partner, pltpu.with_memory_space_constraint(merge_op, pltpu.VMEM))


def transposed_dot(values, merge_op):
    rows, width = values.shape
    return pl.pallas_call(
        transposed_dot_kernel,
        out_shape=jax.ShapeDtypeStruct(values.shape, jnp.bfloat16),
        in_specs=[vmem_spec()] * 2,
        out_specs=vmem_spec(),
        cost_estimate=cost(rows, width),
        compiler_params=pltpu.CompilerParams(vmem_limit_bytes=4 * 1024 * 1024),
    )(values, pltpu.with_memory_space_constraint(merge_op, pltpu.VMEM))


def haar_pair(values, partner, lat_index, bit_level):
    is_lower = lat_index // 2**bit_level % 2 == 0
    first = values.astype(jnp.float32)
    second = partner.astype(jnp.float32)
    return jnp.where(is_lower, (first + second) * half_root, (second - first) * half_root).astype(
        jnp.bfloat16
    )


def level_sign(lat_index, bit_level, width):
    is_lower = lat_index // 2**bit_level % 2 == 0
    return jnp.full((1, width), jnp.where(is_lower, 1.0, -1.0), jnp.float32)


def sweep_layer(leaf_data, merge_op):
    lat_count = lax.axis_size("lat")
    lat_index = lax.axis_index("lat")
    levels = lat_count.bit_length() - 1
    width = leaf_data.shape[1]
    values = leaf_data
    for bit_level in range(levels):
        partner = partner_2(values, "lat", bit_level)
        values = mixed_dot(level_sign(lat_index, bit_level, width), values, partner, merge_op)
    values = transposed_dot(values, merge_op)
    return pushed_down(values, lat_index, lat_count, levels)


def pushed_down(values, lat_index, lat_count, levels):
    gathered = lax.all_gather(values, "lat", axis=0, tiled=False)
    bits = [(lat_index >> level) & 1 for level in range(levels)]
    total = None
    for other in range(lat_count):
        parity = 0
        for level in range(levels):
            if other >> level & 1:
                parity = parity ^ bits[level]
        sign = (1 - 2 * parity).astype(jnp.float32) if other else jnp.float32(1.0)
        term = sign * gathered[other].astype(jnp.float32)
        total = term if total is None else total + term
    return (total * (half_root**levels)).astype(jnp.bfloat16)


def on_device(sources, coupling, merge_ops):
    merge_op = merge_ops[0, 0]
    coupling_row = coupling[0, 0]
    depth_index = lax.axis_index("depth")
    depth_count = lax.axis_size("depth")
    shot_rows = sources[0, 0]
    result = jnp.zeros_like(shot_rows)
    incoming = jnp.zeros_like(shot_rows)
    for sweep_step in range(depth_count):
        leaf_data = (
            shot_rows.astype(jnp.float32) + coupling_row * incoming.astype(jnp.float32)
        ).astype(jnp.bfloat16)
        solved = sweep_layer(leaf_data, merge_op)
        result = jnp.where(depth_index == sweep_step, solved, result)
        if sweep_step + 1 < depth_count:
            incoming = shifted(solved, "depth", 1)
    return result[None, None]


def solution(mesh):
    return jax.shard_map(
        on_device,
        mesh=mesh,
        in_specs=(
            P("depth", "lat", None, None),
            P("depth", "lat", None),
            P("depth", "lat", None, None),
        ),
        out_specs=P("depth", "lat", None, None),
        check_vma=False,
    )
```

```python
import functools

import jax
import jax.numpy as jnp
from jax import lax
from jax.experimental import pallas as pl
from jax.experimental.pallas import tpu as pltpu
from jax.sharding import PartitionSpec as P

half_root = 0.7071067811865476
TILE = 512


def partner_2(block, axis, apart):
    count = lax.axis_size(axis)
    route = []
    for low in range(count):
        high = low | 1 << apart
        if high != low and high < count:
            route += [(low, high), (high, low)]
    return lax.ppermute(block, axis, route)


def shifted(array, axis, by):
    length = lax.axis_size(axis)
    pairs = [(i, i + by) for i in range(length) if 0 <= i + by < length]
    return lax.ppermute(array, axis, pairs)


def mixed_dot_kernel(sign_ref, values_ref, partner_ref, op_ref, out_ref):
    first = values_ref[...].astype(jnp.float32)
    second = partner_ref[...].astype(jnp.float32)
    mixed = ((second + sign_ref[...] * first) * half_root).astype(jnp.bfloat16)
    width = op_ref.shape[1]
    for start in range(0, width, TILE):
        out_ref[:, start:start + TILE] = jnp.dot(
            mixed, op_ref[:, start:start + TILE], preferred_element_type=jnp.float32
        ).astype(out_ref.dtype)


def transposed_dot_kernel(values_ref, op_ref, out_ref):
    values = values_ref[...]
    width = op_ref.shape[0]
    for start in range(0, width, TILE):
        out_ref[:, start:start + TILE] = lax.dot_general(
            values,
            op_ref[start:start + TILE, :],
            (((1,), (1,)), ((), ())),
            preferred_element_type=jnp.float32,
        ).astype(out_ref.dtype)


def vmem_spec():
    return pl.BlockSpec(memory_space=pltpu.VMEM)


def cost(rows, width):
    return pl.CostEstimate(
        flops=2 * rows * width * width,
        bytes_accessed=2 * width * width + 6 * rows * width,
        transcendentals=0,
    )


def mixed_dot(sign, values, partner, merge_op):
    rows, width = values.shape
    return pl.pallas_call(
        mixed_dot_kernel,
        out_shape=jax.ShapeDtypeStruct(values.shape, jnp.bfloat16),
        in_specs=[vmem_spec()] * 4,
        out_specs=vmem_spec(),
        cost_estimate=cost(rows, width),
        compiler_params=pltpu.CompilerParams(vmem_limit_bytes=4 * 1024 * 1024),
    )(sign, values, partner, pltpu.with_memory_space_constraint(merge_op, pltpu.VMEM))


def transposed_dot(values, merge_op):
    rows, width = values.shape
    return pl.pallas_call(
        transposed_dot_kernel,
        out_shape=jax.ShapeDtypeStruct(values.shape, jnp.bfloat16),
        in_specs=[vmem_spec()] * 2,
        out_specs=vmem_spec(),
        cost_estimate=cost(rows, width),
        compiler_params=pltpu.CompilerParams(vmem_limit_bytes=4 * 1024 * 1024),
    )(values, pltpu.with_memory_space_constraint(merge_op, pltpu.VMEM))


def streamed_mixed_kernel(sign_ref, values_ref, partner_ref, op_ref, out_ref, mixed_ref):
    @pl.when(pl.program_id(0) == 0)
    def _():
        first = values_ref[...].astype(jnp.float32)
        second = partner_ref[...].astype(jnp.float32)
        mixed_ref[...] = ((second + sign_ref[...] * first) * half_root).astype(jnp.bfloat16)

    out_ref[...] = jnp.dot(mixed_ref[...], op_ref[...], preferred_element_type=jnp.float32).astype(
        out_ref.dtype
    )


def streamed_transposed_kernel(values_ref, op_ref, out_ref):
    out_ref[...] = lax.dot_general(
        values_ref[...], op_ref[...], (((1,), (1,)), ((), ())), preferred_element_type=jnp.float32
    ).astype(out_ref.dtype)


def whole(shape):
    return pl.BlockSpec(shape, lambda j: (0,) * len(shape))


def streamed_mixed_dot(sign, values, partner, merge_op):
    rows, width = values.shape
    return pl.pallas_call(
        streamed_mixed_kernel,
        out_shape=jax.ShapeDtypeStruct(values.shape, jnp.bfloat16),
        grid=(width // TILE,),
        in_specs=[
            whole(sign.shape),
            whole(values.shape),
            whole(partner.shape),
            pl.BlockSpec((width, TILE), lambda j: (0, j)),
        ],
        out_specs=pl.BlockSpec((rows, TILE), lambda j: (0, j)),
        scratch_shapes=[pltpu.VMEM(values.shape, jnp.bfloat16)],
        cost_estimate=cost(rows, width),
        compiler_params=pltpu.CompilerParams(vmem_limit_bytes=16 * 1024 * 1024),
    )(sign, values, partner, pltpu.with_memory_space_constraint(merge_op, pltpu.HBM))


def streamed_transposed_dot(values, merge_op):
    rows, width = values.shape
    return pl.pallas_call(
        streamed_transposed_kernel,
        out_shape=jax.ShapeDtypeStruct(values.shape, jnp.bfloat16),
        grid=(width // TILE,),
        in_specs=[whole(values.shape), pl.BlockSpec((TILE, width), lambda j: (j, 0))],
        out_specs=pl.BlockSpec((rows, TILE), lambda j: (0, j)),
        cost_estimate=cost(rows, width),
        compiler_params=pltpu.CompilerParams(vmem_limit_bytes=16 * 1024 * 1024),
    )(values, pltpu.with_memory_space_constraint(merge_op, pltpu.HBM))


def haar_pair(values, partner, lat_index, bit_level):
    is_lower = lat_index // 2**bit_level % 2 == 0
    first = values.astype(jnp.float32)
    second = partner.astype(jnp.float32)
    return jnp.where(is_lower, (first + second) * half_root, (second - first) * half_root).astype(
        jnp.bfloat16
    )


def level_sign(lat_index, bit_level, width):
    is_lower = lat_index // 2**bit_level % 2 == 0
    return jnp.full((1, width), jnp.where(is_lower, 1.0, -1.0), jnp.float32)


def sweep_layer(leaf_data, merge_op, streamed):
    lat_count = lax.axis_size("lat")
    lat_index = lax.axis_index("lat")
    levels = lat_count.bit_length() - 1
    width = leaf_data.shape[1]
    values = leaf_data
    for bit_level in range(levels):
        partner = partner_2(values, "lat", bit_level)
        sign = level_sign(lat_index, bit_level, width)
        if streamed:
            values = streamed_mixed_dot(sign, values, partner, merge_op)
        else:
            values = mixed_dot(sign, values, partner, merge_op)
    if streamed:
        values = streamed_transposed_dot(values, merge_op)
    else:
        values = transposed_dot(values, merge_op)
    for bit_level in range(levels - 1, -1, -1):
        partner = partner_2(values, "lat", bit_level)
        values = haar_pair(values, partner, lat_index, bit_level)
    return values


def on_device(sources, coupling, merge_ops):
    merge_op = merge_ops[0, 0]
    coupling_row = coupling[0, 0]
    depth_index = lax.axis_index("depth")
    depth_count = lax.axis_size("depth")
    shot_rows = sources[0, 0]
    result = jnp.zeros_like(shot_rows)
    incoming = jnp.zeros_like(shot_rows)
    for sweep_step in range(depth_count):
        leaf_data = (
            shot_rows.astype(jnp.float32) + coupling_row * incoming.astype(jnp.float32)
        ).astype(jnp.bfloat16)
        solved = sweep_layer(leaf_data, merge_op, sweep_step == 0)
        result = jnp.where(depth_index == sweep_step, solved, result)
        if sweep_step + 1 < depth_count:
            incoming = shifted(solved, "depth", 1)
    return result[None, None]


def solution(mesh):
    return jax.shard_map(
        on_device,
        mesh=mesh,
        in_specs=(
            P("depth", "lat", None, None),
            P("depth", "lat", None),
            P("depth", "lat", None, None),
        ),
        out_specs=P("depth", "lat", None, None),
        check_vma=False,
    )
```

```python
import functools

import jax
import jax.numpy as jnp
from jax import lax
from jax.experimental import pallas as pl
from jax.experimental.pallas import tpu as pltpu
from jax.sharding import PartitionSpec as P

half_root = 0.7071067811865476
TILE = 512


def partner_2(block, axis, apart):
    count = lax.axis_size(axis)
    route = []
    for low in range(count):
        high = low | 1 << apart
        if high != low and high < count:
            route += [(low, high), (high, low)]
    return lax.ppermute(block, axis, route)


def shifted(array, axis, by):
    length = lax.axis_size(axis)
    pairs = [(i, i + by) for i in range(length) if 0 <= i + by < length]
    return lax.ppermute(array, axis, pairs)


def mixed_dot_kernel(sign_ref, values_ref, partner_ref, op_ref, out_ref):
    first = values_ref[...].astype(jnp.float32)
    second = partner_ref[...].astype(jnp.float32)
    mixed = ((second + sign_ref[...] * first) * half_root).astype(jnp.bfloat16)
    width = op_ref.shape[1]
    for start in range(0, width, TILE):
        out_ref[:, start:start + TILE] = jnp.dot(
            mixed, op_ref[:, start:start + TILE], preferred_element_type=jnp.float32
        ).astype(out_ref.dtype)


def transposed_dot_kernel(values_ref, op_ref, out_ref):
    values = values_ref[...]
    width = op_ref.shape[0]
    for start in range(0, width, TILE):
        out_ref[:, start:start + TILE] = lax.dot_general(
            values,
            op_ref[start:start + TILE, :],
            (((1,), (1,)), ((), ())),
            preferred_element_type=jnp.float32,
        ).astype(out_ref.dtype)


def vmem_spec():
    return pl.BlockSpec(memory_space=pltpu.VMEM)


def cost(rows, width):
    return pl.CostEstimate(
        flops=2 * rows * width * width,
        bytes_accessed=2 * width * width + 6 * rows * width,
        transcendentals=0,
    )


def mixed_dot(sign, values, partner, merge_op):
    rows, width = values.shape
    return pl.pallas_call(
        mixed_dot_kernel,
        out_shape=jax.ShapeDtypeStruct(values.shape, jnp.bfloat16),
        in_specs=[vmem_spec()] * 4,
        out_specs=vmem_spec(),
        cost_estimate=cost(rows, width),
        compiler_params=pltpu.CompilerParams(vmem_limit_bytes=4 * 1024 * 1024),
    )(sign, values, partner, pltpu.with_memory_space_constraint(merge_op, pltpu.VMEM))


def transposed_dot(values, merge_op):
    rows, width = values.shape
    return pl.pallas_call(
        transposed_dot_kernel,
        out_shape=jax.ShapeDtypeStruct(values.shape, jnp.bfloat16),
        in_specs=[vmem_spec()] * 2,
        out_specs=vmem_spec(),
        cost_estimate=cost(rows, width),
        compiler_params=pltpu.CompilerParams(vmem_limit_bytes=4 * 1024 * 1024),
    )(values, pltpu.with_memory_space_constraint(merge_op, pltpu.VMEM))


def haar_pair(values, partner, lat_index, bit_level):
    is_lower = lat_index // 2**bit_level % 2 == 0
    first = values.astype(jnp.float32)
    second = partner.astype(jnp.float32)
    return jnp.where(is_lower, (first + second) * half_root, (second - first) * half_root).astype(
        jnp.bfloat16
    )


def level_sign(lat_index, bit_level, width):
    is_lower = lat_index // 2**bit_level % 2 == 0
    return jnp.full((1, width), jnp.where(is_lower, 1.0, -1.0), jnp.float32)


def sweep_layer(leaf_data, partner_leaf, merge_op):
    lat_count = lax.axis_size("lat")
    lat_index = lax.axis_index("lat")
    levels = lat_count.bit_length() - 1
    width = leaf_data.shape[1]
    values = leaf_data
    for bit_level in range(levels):
        partner = partner_leaf if bit_level == 0 else partner_2(values, "lat", bit_level)
        values = mixed_dot(level_sign(lat_index, bit_level, width), values, partner, merge_op)
    values = transposed_dot(values, merge_op)
    for bit_level in range(levels - 1, 0, -1):
        partner = partner_2(values, "lat", bit_level)
        values = haar_pair(values, partner, lat_index, bit_level)
    return values


def on_device(sources, coupling, merge_ops):
    merge_op = merge_ops[0, 0]
    coupling_row = coupling[0, 0]
    depth_index = lax.axis_index("depth")
    depth_count = lax.axis_size("depth")
    lat_index = lax.axis_index("lat")
    shot_rows = sources[0, 0]
    partner_rows = partner_2(shot_rows, "lat", 0)
    partner_coupling = partner_2(coupling_row[None], "lat", 0)[0]
    result = jnp.zeros_like(shot_rows)
    incoming = jnp.zeros_like(shot_rows)
    partner_incoming = jnp.zeros_like(shot_rows)
    for sweep_step in range(depth_count):
        leaf_data = (
            shot_rows.astype(jnp.float32) + coupling_row * incoming.astype(jnp.float32)
        ).astype(jnp.bfloat16)
        partner_leaf = (
            partner_rows.astype(jnp.float32) + partner_coupling * partner_incoming.astype(jnp.float32)
        ).astype(jnp.bfloat16)
        level_one = sweep_layer(leaf_data, partner_leaf, merge_op)
        if sweep_step + 1 < depth_count:
            arrived = shifted(level_one, "depth", 1)
            level_one = jnp.where(depth_index == sweep_step, level_one, arrived)
        other = partner_2(level_one, "lat", 0)
        solved = haar_pair(level_one, other, lat_index, 0)
        partner_solved = haar_pair(other, level_one, lat_index ^ 1, 0)
        result = jnp.where(depth_index == sweep_step, solved, result)
        incoming = solved
        partner_incoming = partner_solved
    return result[None, None]


def solution(mesh):
    return jax.shard_map(
        on_device,
        mesh=mesh,
        in_specs=(
            P("depth", "lat", None, None),
            P("depth", "lat", None),
            P("depth", "lat", None, None),
        ),
        out_specs=P("depth", "lat", None, None),
        check_vma=False,
    )
```

```python
import functools

import jax
import jax.numpy as jnp
from jax import lax
from jax.experimental import pallas as pl
from jax.experimental.pallas import tpu as pltpu
from jax.sharding import PartitionSpec as P

half_root = 0.7071067811865476
TILE = 512


def partner_2(block, axis, apart):
    count = lax.axis_size(axis)
    route = []
    for low in range(count):
        high = low | 1 << apart
        if high != low and high < count:
            route += [(low, high), (high, low)]
    return lax.ppermute(block, axis, route)


def handed_down(array, axis, layer):
    return lax.ppermute(array, axis, [(layer, layer + 1)])


def mixed_dot_kernel(sign_ref, values_ref, partner_ref, op_ref, out_ref):
    first = values_ref[...].astype(jnp.float32)
    second = partner_ref[...].astype(jnp.float32)
    mixed = ((second + sign_ref[...] * first) * half_root).astype(jnp.bfloat16)
    width = op_ref.shape[1]
    for start in range(0, width, TILE):
        out_ref[:, start:start + TILE] = jnp.dot(
            mixed, op_ref[:, start:start + TILE], preferred_element_type=jnp.float32
        ).astype(out_ref.dtype)


def transposed_dot_kernel(values_ref, op_ref, out_ref):
    values = values_ref[...]
    width = op_ref.shape[0]
    for start in range(0, width, TILE):
        out_ref[:, start:start + TILE] = lax.dot_general(
            values,
            op_ref[start:start + TILE, :],
            (((1,), (1,)), ((), ())),
            preferred_element_type=jnp.float32,
        ).astype(out_ref.dtype)


def vmem_spec():
    return pl.BlockSpec(memory_space=pltpu.VMEM)


def cost(rows, width):
    return pl.CostEstimate(
        flops=2 * rows * width * width,
        bytes_accessed=2 * width * width + 6 * rows * width,
        transcendentals=0,
    )


def mixed_dot(sign, values, partner, merge_op):
    rows, width = values.shape
    return pl.pallas_call(
        mixed_dot_kernel,
        out_shape=jax.ShapeDtypeStruct(values.shape, jnp.bfloat16),
        in_specs=[vmem_spec()] * 4,
        out_specs=vmem_spec(),
        cost_estimate=cost(rows, width),
        compiler_params=pltpu.CompilerParams(vmem_limit_bytes=4 * 1024 * 1024),
    )(sign, values, partner, pltpu.with_memory_space_constraint(merge_op, pltpu.VMEM))


def transposed_dot(values, merge_op):
    rows, width = values.shape
    return pl.pallas_call(
        transposed_dot_kernel,
        out_shape=jax.ShapeDtypeStruct(values.shape, jnp.bfloat16),
        in_specs=[vmem_spec()] * 2,
        out_specs=vmem_spec(),
        cost_estimate=cost(rows, width),
        compiler_params=pltpu.CompilerParams(vmem_limit_bytes=4 * 1024 * 1024),
    )(values, pltpu.with_memory_space_constraint(merge_op, pltpu.VMEM))


def haar_pair(values, partner, lat_index, bit_level):
    is_lower = lat_index // 2**bit_level % 2 == 0
    first = values.astype(jnp.float32)
    second = partner.astype(jnp.float32)
    return jnp.where(is_lower, (first + second) * half_root, (second - first) * half_root).astype(
        jnp.bfloat16
    )


def level_sign(lat_index, bit_level, width):
    is_lower = lat_index // 2**bit_level % 2 == 0
    return jnp.full((1, width), jnp.where(is_lower, 1.0, -1.0), jnp.float32)


def sweep_layer(leaf_data, merge_op):
    lat_count = lax.axis_size("lat")
    lat_index = lax.axis_index("lat")
    levels = lat_count.bit_length() - 1
    width = leaf_data.shape[1]
    values = leaf_data
    for bit_level in range(levels):
        partner = partner_2(values, "lat", bit_level)
        values = mixed_dot(level_sign(lat_index, bit_level, width), values, partner, merge_op)
    values = transposed_dot(values, merge_op)
    for bit_level in range(levels - 1, -1, -1):
        partner = partner_2(values, "lat", bit_level)
        values = haar_pair(values, partner, lat_index, bit_level)
    return values


def on_device(sources, coupling, merge_ops):
    merge_op = merge_ops[0, 0]
    coupling_row = coupling[0, 0]
    depth_index = lax.axis_index("depth")
    depth_count = lax.axis_size("depth")
    shot_rows = sources[0, 0]
    result = jnp.zeros_like(shot_rows)
    incoming = jnp.zeros_like(shot_rows)
    for sweep_step in range(depth_count):
        leaf_data = (
            shot_rows.astype(jnp.float32) + coupling_row * incoming.astype(jnp.float32)
        ).astype(jnp.bfloat16)
        solved = sweep_layer(leaf_data, merge_op)
        result = jnp.where(depth_index == sweep_step, solved, result)
        if sweep_step + 1 < depth_count:
            incoming = handed_down(solved, "depth", sweep_step)
    return result[None, None]


def solution(mesh):
    return jax.shard_map(
        on_device,
        mesh=mesh,
        in_specs=(
            P("depth", "lat", None, None),
            P("depth", "lat", None),
            P("depth", "lat", None, None),
        ),
        out_specs=P("depth", "lat", None, None),
        check_vma=False,
    )
```

```python
import functools

import jax
import jax.numpy as jnp
from jax import lax
from jax.experimental import pallas as pl
from jax.experimental.pallas import tpu as pltpu
from jax.sharding import PartitionSpec as P

half_root = 0.7071067811865476
TILE = 512


def partner_2(block, axis, apart):
    count = lax.axis_size(axis)
    route = []
    for low in range(count):
        high = low | 1 << apart
        if high != low and high < count:
            route += [(low, high), (high, low)]
    return lax.ppermute(block, axis, route)


def handed_down(array, axis, layer):
    return lax.ppermute(array, axis, [(layer, layer + 1)])


def mixed_dot_kernel(sign_ref, values_ref, partner_ref, op_ref, out_ref):
    first = values_ref[...].astype(jnp.float32)
    second = partner_ref[...].astype(jnp.float32)
    mixed = ((second + sign_ref[...] * first) * half_root).astype(jnp.bfloat16)
    width = op_ref.shape[1]
    for start in range(0, width, TILE):
        out_ref[:, start:start + TILE] = jnp.dot(
            mixed, op_ref[:, start:start + TILE], preferred_element_type=jnp.float32
        ).astype(out_ref.dtype)


def transposed_dot_kernel(values_ref, op_ref, out_ref):
    values = values_ref[...]
    width = op_ref.shape[0]
    for start in range(0, width, TILE):
        out_ref[:, start:start + TILE] = lax.dot_general(
            values,
            op_ref[start:start + TILE, :],
            (((1,), (1,)), ((), ())),
            preferred_element_type=jnp.float32,
        ).astype(out_ref.dtype)


def vmem_spec():
    return pl.BlockSpec(memory_space=pltpu.VMEM)


def cost(rows, width):
    return pl.CostEstimate(
        flops=2 * rows * width * width,
        bytes_accessed=2 * width * width + 6 * rows * width,
        transcendentals=0,
    )


def mixed_dot(sign, values, partner, merge_op):
    rows, width = values.shape
    return pl.pallas_call(
        mixed_dot_kernel,
        out_shape=jax.ShapeDtypeStruct(values.shape, jnp.bfloat16),
        in_specs=[vmem_spec()] * 4,
        out_specs=vmem_spec(),
        cost_estimate=cost(rows, width),
        compiler_params=pltpu.CompilerParams(vmem_limit_bytes=4 * 1024 * 1024),
    )(sign, values, partner, pltpu.with_memory_space_constraint(merge_op, pltpu.VMEM))


def transposed_dot(values, merge_op):
    rows, width = values.shape
    return pl.pallas_call(
        transposed_dot_kernel,
        out_shape=jax.ShapeDtypeStruct(values.shape, jnp.bfloat16),
        in_specs=[vmem_spec()] * 2,
        out_specs=vmem_spec(),
        cost_estimate=cost(rows, width),
        compiler_params=pltpu.CompilerParams(vmem_limit_bytes=4 * 1024 * 1024),
    )(values, pltpu.with_memory_space_constraint(merge_op, pltpu.VMEM))


CHUNK = 256


def fetched_dot_kernel(mix, *refs):
    if mix:
        sign_ref, values_ref, partner_ref, op_hbm_ref, out_ref, op_ref, sems = refs
    else:
        values_ref, op_hbm_ref, out_ref, op_ref, sems = refs
    width = op_ref.shape[0]
    copies = []
    for index in range(width // CHUNK):
        rows = pl.ds(index * CHUNK, CHUNK)
        copy = pltpu.make_async_copy(op_hbm_ref.at[rows, :], op_ref.at[rows, :], sems.at[index])
        copy.start()
        copies.append(copy)
    if mix:
        first = values_ref[...].astype(jnp.float32)
        second = partner_ref[...].astype(jnp.float32)
        mixed = ((second + sign_ref[...] * first) * half_root).astype(jnp.bfloat16)
        total = jnp.zeros(out_ref.shape, jnp.float32)
        for index, copy in enumerate(copies):
            copy.wait()
            rows = slice(index * CHUNK, (index + 1) * CHUNK)
            total = total + jnp.dot(mixed[:, rows], op_ref[rows, :], preferred_element_type=jnp.float32)
        out_ref[...] = total.astype(out_ref.dtype)
    else:
        values = values_ref[...]
        for index, copy in enumerate(copies):
            copy.wait()
            rows = slice(index * CHUNK, (index + 1) * CHUNK)
            out_ref[:, rows] = lax.dot_general(
                values, op_ref[rows, :], (((1,), (1,)), ((), ())), preferred_element_type=jnp.float32
            ).astype(out_ref.dtype)


def fetched_dot(operands, merge_op, mix):
    values = operands[1] if mix else operands[0]
    rows, width = values.shape
    return pl.pallas_call(
        functools.partial(fetched_dot_kernel, mix),
        out_shape=jax.ShapeDtypeStruct(values.shape, jnp.bfloat16),
        in_specs=[vmem_spec()] * len(operands) + [pl.BlockSpec(memory_space=pl.ANY)],
        out_specs=vmem_spec(),
        scratch_shapes=[
            pltpu.VMEM(merge_op.shape, merge_op.dtype),
            pltpu.SemaphoreType.DMA((width // CHUNK,)),
        ],
        cost_estimate=cost(rows, width),
        compiler_params=pltpu.CompilerParams(vmem_limit_bytes=16 * 1024 * 1024),
    )(*operands, pltpu.with_memory_space_constraint(merge_op, pltpu.HBM))


def haar_pair(values, partner, lat_index, bit_level):
    is_lower = lat_index // 2**bit_level % 2 == 0
    first = values.astype(jnp.float32)
    second = partner.astype(jnp.float32)
    return jnp.where(is_lower, (first + second) * half_root, (second - first) * half_root).astype(
        jnp.bfloat16
    )


def level_sign(lat_index, bit_level, width):
    is_lower = lat_index // 2**bit_level % 2 == 0
    return jnp.full((1, width), jnp.where(is_lower, 1.0, -1.0), jnp.float32)


def sweep_layer(leaf_data, merge_op, fetch):
    lat_count = lax.axis_size("lat")
    lat_index = lax.axis_index("lat")
    levels = lat_count.bit_length() - 1
    width = leaf_data.shape[1]
    values = leaf_data
    for bit_level in range(levels):
        partner = partner_2(values, "lat", bit_level)
        sign = level_sign(lat_index, bit_level, width)
        if fetch:
            values = fetched_dot((sign, values, partner), merge_op, True)
        else:
            values = mixed_dot(sign, values, partner, merge_op)
    if fetch:
        values = fetched_dot((values,), merge_op, False)
    else:
        values = transposed_dot(values, merge_op)
    for bit_level in range(levels - 1, -1, -1):
        partner = partner_2(values, "lat", bit_level)
        values = haar_pair(values, partner, lat_index, bit_level)
    return values


def on_device(sources, coupling, merge_ops):
    merge_op = merge_ops[0, 0]
    coupling_row = coupling[0, 0]
    depth_index = lax.axis_index("depth")
    depth_count = lax.axis_size("depth")
    shot_rows = sources[0, 0]
    result = jnp.zeros_like(shot_rows)
    incoming = jnp.zeros_like(shot_rows)
    for sweep_step in range(depth_count):
        leaf_data = (
            shot_rows.astype(jnp.float32) + coupling_row * incoming.astype(jnp.float32)
        ).astype(jnp.bfloat16)
        solved = sweep_layer(leaf_data, merge_op, sweep_step == 0)
        result = jnp.where(depth_index == sweep_step, solved, result)
        if sweep_step + 1 < depth_count:
            incoming = handed_down(solved, "depth", sweep_step)
    return result[None, None]


def solution(mesh):
    return jax.shard_map(
        on_device,
        mesh=mesh,
        in_specs=(
            P("depth", "lat", None, None),
            P("depth", "lat", None),
            P("depth", "lat", None, None),
        ),
        out_specs=P("depth", "lat", None, None),
        check_vma=False,
    )
```

```python
import functools

import jax
import jax.numpy as jnp
from jax import lax
from jax.experimental import pallas as pl
from jax.experimental.pallas import tpu as pltpu
from jax.sharding import PartitionSpec as P

half_root = 0.7071067811865476
TILE = 512


def partner_2(block, axis, apart, layer):
    count = lax.axis_size(axis)
    route = []
    for low in range(count):
        high = low | 1 << apart
        if high != low and high < count:
            route += [(layer * count + low, layer * count + high), (layer * count + high, layer * count + low)]
    return lax.ppermute(block, ("depth", axis), route)


def handed_down(array, axis, layer):
    return lax.ppermute(array, axis, [(layer, layer + 1)])


def mixed_dot_kernel(sign_ref, values_ref, partner_ref, op_ref, out_ref):
    first = values_ref[...].astype(jnp.float32)
    second = partner_ref[...].astype(jnp.float32)
    mixed = ((second + sign_ref[...] * first) * half_root).astype(jnp.bfloat16)
    width = op_ref.shape[1]
    for start in range(0, width, TILE):
        out_ref[:, start:start + TILE] = jnp.dot(
            mixed, op_ref[:, start:start + TILE], preferred_element_type=jnp.float32
        ).astype(out_ref.dtype)


def transposed_dot_kernel(values_ref, op_ref, out_ref):
    values = values_ref[...]
    width = op_ref.shape[0]
    for start in range(0, width, TILE):
        out_ref[:, start:start + TILE] = lax.dot_general(
            values,
            op_ref[start:start + TILE, :],
            (((1,), (1,)), ((), ())),
            preferred_element_type=jnp.float32,
        ).astype(out_ref.dtype)


def vmem_spec():
    return pl.BlockSpec(memory_space=pltpu.VMEM)


def cost(rows, width):
    return pl.CostEstimate(
        flops=2 * rows * width * width,
        bytes_accessed=2 * width * width + 6 * rows * width,
        transcendentals=0,
    )


def mixed_dot(sign, values, partner, merge_op):
    rows, width = values.shape
    return pl.pallas_call(
        mixed_dot_kernel,
        out_shape=jax.ShapeDtypeStruct(values.shape, jnp.bfloat16),
        in_specs=[vmem_spec()] * 4,
        out_specs=vmem_spec(),
        cost_estimate=cost(rows, width),
        compiler_params=pltpu.CompilerParams(vmem_limit_bytes=4 * 1024 * 1024),
    )(sign, values, partner, pltpu.with_memory_space_constraint(merge_op, pltpu.VMEM))


def transposed_dot(values, merge_op):
    rows, width = values.shape
    return pl.pallas_call(
        transposed_dot_kernel,
        out_shape=jax.ShapeDtypeStruct(values.shape, jnp.bfloat16),
        in_specs=[vmem_spec()] * 2,
        out_specs=vmem_spec(),
        cost_estimate=cost(rows, width),
        compiler_params=pltpu.CompilerParams(vmem_limit_bytes=4 * 1024 * 1024),
    )(values, pltpu.with_memory_space_constraint(merge_op, pltpu.VMEM))


def haar_pair(values, partner, lat_index, bit_level):
    is_lower = lat_index // 2**bit_level % 2 == 0
    first = values.astype(jnp.float32)
    second = partner.astype(jnp.float32)
    return jnp.where(is_lower, (first + second) * half_root, (second - first) * half_root).astype(
        jnp.bfloat16
    )


def level_sign(lat_index, bit_level, width):
    is_lower = lat_index // 2**bit_level % 2 == 0
    return jnp.full((1, width), jnp.where(is_lower, 1.0, -1.0), jnp.float32)


def sweep_layer(leaf_data, merge_op, layer):
    lat_count = lax.axis_size("lat")
    lat_index = lax.axis_index("lat")
    levels = lat_count.bit_length() - 1
    width = leaf_data.shape[1]
    values = leaf_data
    for bit_level in range(levels):
        partner = partner_2(values, "lat", bit_level, layer)
        values = mixed_dot(level_sign(lat_index, bit_level, width), values, partner, merge_op)
    values = transposed_dot(values, merge_op)
    for bit_level in range(levels - 1, -1, -1):
        partner = partner_2(values, "lat", bit_level, layer)
        values = haar_pair(values, partner, lat_index, bit_level)
    return values


def on_device(sources, coupling, merge_ops):
    merge_op = merge_ops[0, 0]
    coupling_row = coupling[0, 0]
    depth_index = lax.axis_index("depth")
    depth_count = lax.axis_size("depth")
    shot_rows = sources[0, 0]
    result = jnp.zeros_like(shot_rows)
    incoming = jnp.zeros_like(shot_rows)
    for sweep_step in range(depth_count):
        leaf_data = (
            shot_rows.astype(jnp.float32) + coupling_row * incoming.astype(jnp.float32)
        ).astype(jnp.bfloat16)
        solved = sweep_layer(leaf_data, merge_op, sweep_step)
        result = jnp.where(depth_index == sweep_step, solved, result)
        if sweep_step + 1 < depth_count:
            incoming = handed_down(solved, "depth", sweep_step)
    return result[None, None]


def solution(mesh):
    return jax.shard_map(
        on_device,
        mesh=mesh,
        in_specs=(
            P("depth", "lat", None, None),
            P("depth", "lat", None),
            P("depth", "lat", None, None),
        ),
        out_specs=P("depth", "lat", None, None),
        check_vma=False,
    )
```

```python
import functools

import jax
import jax.numpy as jnp
from jax import lax
from jax.experimental import pallas as pl
from jax.experimental.pallas import tpu as pltpu
from jax.sharding import PartitionSpec as P

half_root = 0.7071067811865476
TILE = 512


def partner_2(block, axis, apart):
    count = lax.axis_size(axis)
    route = []
    for low in range(count):
        high = low | 1 << apart
        if high != low and high < count:
            route += [(low, high), (high, low)]
    return lax.ppermute(block, axis, route)


def handed_down(array, axis, layer):
    return lax.ppermute(array, axis, [(layer, layer + 1)])


def mixed_dot_kernel(sign_ref, values_ref, partner_ref, op_ref, out_ref):
    first = values_ref[...].astype(jnp.float32)
    second = partner_ref[...].astype(jnp.float32)
    mixed = ((second + sign_ref[...] * first) * half_root).astype(jnp.bfloat16)
    width = op_ref.shape[1]
    for start in range(0, width, TILE):
        out_ref[:, start:start + TILE] = jnp.dot(
            mixed, op_ref[:, start:start + TILE], preferred_element_type=jnp.float32
        ).astype(out_ref.dtype)


def transposed_dot_kernel(values_ref, op_ref, out_ref):
    values = values_ref[...]
    width = op_ref.shape[0]
    for start in range(0, width, TILE):
        out_ref[:, start:start + TILE] = lax.dot_general(
            values,
            op_ref[start:start + TILE, :],
            (((1,), (1,)), ((), ())),
            preferred_element_type=jnp.float32,
        ).astype(out_ref.dtype)


def vmem_spec():
    return pl.BlockSpec(memory_space=pltpu.VMEM)


def cost(rows, width):
    return pl.CostEstimate(
        flops=2 * rows * width * width,
        bytes_accessed=2 * width * width + 6 * rows * width,
        transcendentals=0,
    )


def mixed_dot(sign, values, partner, merge_op):
    rows, width = values.shape
    return pl.pallas_call(
        mixed_dot_kernel,
        out_shape=jax.ShapeDtypeStruct(values.shape, jnp.bfloat16),
        in_specs=[vmem_spec()] * 4,
        out_specs=vmem_spec(),
        cost_estimate=cost(rows, width),
        compiler_params=pltpu.CompilerParams(vmem_limit_bytes=4 * 1024 * 1024),
    )(sign, values, partner, pltpu.with_memory_space_constraint(merge_op, pltpu.VMEM))


def transposed_dot(values, merge_op):
    rows, width = values.shape
    return pl.pallas_call(
        transposed_dot_kernel,
        out_shape=jax.ShapeDtypeStruct(values.shape, jnp.bfloat16),
        in_specs=[vmem_spec()] * 2,
        out_specs=vmem_spec(),
        cost_estimate=cost(rows, width),
        compiler_params=pltpu.CompilerParams(vmem_limit_bytes=4 * 1024 * 1024),
    )(values, pltpu.with_memory_space_constraint(merge_op, pltpu.VMEM))


def haar_pair(values, partner, lat_index, bit_level):
    is_lower = lat_index // 2**bit_level % 2 == 0
    first = values.astype(jnp.float32)
    second = partner.astype(jnp.float32)
    return jnp.where(is_lower, (first + second) * half_root, (second - first) * half_root).astype(
        jnp.bfloat16
    )


def level_sign(lat_index, bit_level, width):
    is_lower = lat_index // 2**bit_level % 2 == 0
    return jnp.full((1, width), jnp.where(is_lower, 1.0, -1.0), jnp.float32)


def sweep_layer(leaf_data, merge_op):
    lat_count = lax.axis_size("lat")
    lat_index = lax.axis_index("lat")
    levels = lat_count.bit_length() - 1
    width = leaf_data.shape[1]
    values = leaf_data
    for bit_level in range(levels):
        partner = partner_2(values, "lat", bit_level)
        values = mixed_dot(level_sign(lat_index, bit_level, width), values, partner, merge_op)
    values = transposed_dot(values, merge_op)
    for bit_level in range(levels - 1, -1, -1):
        partner = partner_2(values, "lat", bit_level)
        values = haar_pair(values, partner, lat_index, bit_level)
    return values


def on_device(sources, coupling, merge_ops):
    merge_op = merge_ops[0, 0]
    coupling_row = coupling[0, 0]
    depth_index = lax.axis_index("depth")
    depth_count = lax.axis_size("depth")
    shot_rows = sources[0, 0]
    result = jnp.zeros_like(shot_rows)
    for sweep_step in range(depth_count):
        if sweep_step == 0:
            leaf_data = shot_rows
        else:
            leaf_data = (
                shot_rows.astype(jnp.float32) + coupling_row * incoming.astype(jnp.float32)
            ).astype(jnp.bfloat16)
        solved = sweep_layer(leaf_data, merge_op)
        result = jnp.where(depth_index == sweep_step, solved, result)
        if sweep_step + 1 < depth_count:
            incoming = handed_down(solved, "depth", sweep_step)
    return result[None, None]


def solution(mesh):
    return jax.shard_map(
        on_device,
        mesh=mesh,
        in_specs=(
            P("depth", "lat", None, None),
            P("depth", "lat", None),
            P("depth", "lat", None, None),
        ),
        out_specs=P("depth", "lat", None, None),
        check_vma=False,
    )
```

```python
import functools

import jax
import jax.numpy as jnp
from jax import lax
from jax.experimental import pallas as pl
from jax.experimental.pallas import tpu as pltpu
from jax.sharding import PartitionSpec as P

half_root = 0.7071067811865476
TILE = 512


def partner_2(block, axis, apart):
    count = lax.axis_size(axis)
    route = []
    for low in range(count):
        high = low | 1 << apart
        if high != low and high < count:
            route += [(low, high), (high, low)]
    return lax.ppermute(block, axis, route)


def handed_down(array, axis, layer):
    return lax.ppermute(array, axis, [(layer, layer + 1)])


def mixed_dot_kernel(sign_ref, values_ref, partner_ref, op_ref, out_ref):
    first = values_ref[...].astype(jnp.float32)
    second = partner_ref[...].astype(jnp.float32)
    mixed = ((second + sign_ref[...] * first) * half_root).astype(jnp.bfloat16)
    width = op_ref.shape[1]
    for start in range(0, width, TILE):
        out_ref[:, start:start + TILE] = jnp.dot(
            mixed, op_ref[:, start:start + TILE], preferred_element_type=jnp.float32
        ).astype(out_ref.dtype)


def transposed_dot_kernel(values_ref, op_ref, out_ref):
    values = values_ref[...]
    width = op_ref.shape[0]
    for start in range(0, width, TILE):
        out_ref[:, start:start + TILE] = lax.dot_general(
            values,
            op_ref[start:start + TILE, :],
            (((1,), (1,)), ((), ())),
            preferred_element_type=jnp.float32,
        ).astype(out_ref.dtype)


def vmem_spec():
    return pl.BlockSpec(memory_space=pltpu.VMEM)


def cost(rows, width):
    return pl.CostEstimate(
        flops=2 * rows * width * width,
        bytes_accessed=2 * width * width + 6 * rows * width,
        transcendentals=0,
    )


def mixed_dot(sign, values, partner, merge_op):
    rows, width = values.shape
    return pl.pallas_call(
        mixed_dot_kernel,
        out_shape=jax.ShapeDtypeStruct(values.shape, jnp.bfloat16),
        in_specs=[vmem_spec()] * 4,
        out_specs=vmem_spec(),
        cost_estimate=cost(rows, width),
        compiler_params=pltpu.CompilerParams(vmem_limit_bytes=4 * 1024 * 1024),
    )(sign, values, partner, pltpu.with_memory_space_constraint(merge_op, pltpu.VMEM))


def transposed_dot(values, merge_op):
    rows, width = values.shape
    return pl.pallas_call(
        transposed_dot_kernel,
        out_shape=jax.ShapeDtypeStruct(values.shape, jnp.bfloat16),
        in_specs=[vmem_spec()] * 2,
        out_specs=vmem_spec(),
        cost_estimate=cost(rows, width),
        compiler_params=pltpu.CompilerParams(vmem_limit_bytes=4 * 1024 * 1024),
    )(values, pltpu.with_memory_space_constraint(merge_op, pltpu.VMEM))


CHUNK = 256


def fetched_dot_kernel(mix, *refs):
    if mix:
        sign_ref, values_ref, partner_ref, op_hbm_ref, out_ref, op_ref, sems = refs
    else:
        values_ref, op_hbm_ref, out_ref, op_ref, sems = refs
    width = op_ref.shape[0]
    copies = []
    for index in range(width // CHUNK):
        rows = pl.ds(index * CHUNK, CHUNK)
        copy = pltpu.make_async_copy(op_hbm_ref.at[rows, :], op_ref.at[rows, :], sems.at[index])
        copy.start()
        copies.append(copy)
    if mix:
        first = values_ref[...].astype(jnp.float32)
        second = partner_ref[...].astype(jnp.float32)
        mixed = ((second + sign_ref[...] * first) * half_root).astype(jnp.bfloat16)
        total = jnp.zeros(out_ref.shape, jnp.float32)
        for index, copy in enumerate(copies):
            copy.wait()
            rows = slice(index * CHUNK, (index + 1) * CHUNK)
            total = total + jnp.dot(mixed[:, rows], op_ref[rows, :], preferred_element_type=jnp.float32)
        out_ref[...] = total.astype(out_ref.dtype)
    else:
        values = values_ref[...]
        for index, copy in enumerate(copies):
            copy.wait()
            rows = slice(index * CHUNK, (index + 1) * CHUNK)
            out_ref[:, rows] = lax.dot_general(
                values, op_ref[rows, :], (((1,), (1,)), ((), ())), preferred_element_type=jnp.float32
            ).astype(out_ref.dtype)


def fetched_dot(operands, merge_op, mix):
    values = operands[1] if mix else operands[0]
    rows, width = values.shape
    return pl.pallas_call(
        functools.partial(fetched_dot_kernel, mix),
        out_shape=jax.ShapeDtypeStruct(values.shape, jnp.bfloat16),
        in_specs=[vmem_spec()] * len(operands) + [pl.BlockSpec(memory_space=pl.ANY)],
        out_specs=vmem_spec(),
        scratch_shapes=[
            pltpu.VMEM(merge_op.shape, merge_op.dtype),
            pltpu.SemaphoreType.DMA((width // CHUNK,)),
        ],
        cost_estimate=cost(rows, width),
        compiler_params=pltpu.CompilerParams(vmem_limit_bytes=16 * 1024 * 1024),
    )(*operands, pltpu.with_memory_space_constraint(merge_op, pltpu.HBM))


def haar_pair(values, partner, lat_index, bit_level):
    is_lower = lat_index // 2**bit_level % 2 == 0
    first = values.astype(jnp.float32)
    second = partner.astype(jnp.float32)
    return jnp.where(is_lower, (first + second) * half_root, (second - first) * half_root).astype(
        jnp.bfloat16
    )


def level_sign(lat_index, bit_level, width):
    is_lower = lat_index // 2**bit_level % 2 == 0
    return jnp.full((1, width), jnp.where(is_lower, 1.0, -1.0), jnp.float32)


def sweep_layer(leaf_data, merge_op, fetch):
    lat_count = lax.axis_size("lat")
    lat_index = lax.axis_index("lat")
    levels = lat_count.bit_length() - 1
    width = leaf_data.shape[1]
    values = leaf_data
    for bit_level in range(levels):
        partner = partner_2(values, "lat", bit_level)
        sign = level_sign(lat_index, bit_level, width)
        if fetch and bit_level < levels - 1:
            values = fetched_dot((sign, values, partner), merge_op, True)
        else:
            values = mixed_dot(sign, values, partner, merge_op)
    values = transposed_dot(values, merge_op)
    for bit_level in range(levels - 1, -1, -1):
        partner = partner_2(values, "lat", bit_level)
        values = haar_pair(values, partner, lat_index, bit_level)
    return values


def on_device(sources, coupling, merge_ops):
    merge_op = merge_ops[0, 0]
    coupling_row = coupling[0, 0]
    depth_index = lax.axis_index("depth")
    depth_count = lax.axis_size("depth")
    shot_rows = sources[0, 0]
    result = jnp.zeros_like(shot_rows)
    for sweep_step in range(depth_count):
        if sweep_step == 0:
            leaf_data = shot_rows
        else:
            leaf_data = (
                shot_rows.astype(jnp.float32) + coupling_row * incoming.astype(jnp.float32)
            ).astype(jnp.bfloat16)
        solved = sweep_layer(leaf_data, merge_op, sweep_step == 0)
        result = jnp.where(depth_index == sweep_step, solved, result)
        if sweep_step + 1 < depth_count:
            incoming = handed_down(solved, "depth", sweep_step)
    return result[None, None]


def solution(mesh):
    return jax.shard_map(
        on_device,
        mesh=mesh,
        in_specs=(
            P("depth", "lat", None, None),
            P("depth", "lat", None),
            P("depth", "lat", None, None),
        ),
        out_specs=P("depth", "lat", None, None),
        check_vma=False,
    )
```

```python
import functools

import jax
import jax.numpy as jnp
from jax import lax
from jax.experimental import pallas as pl
from jax.experimental.pallas import tpu as pltpu
from jax.sharding import PartitionSpec as P

half_root = 0.7071067811865476
TILE = 512


def partner_2(block, axis, apart):
    count = lax.axis_size(axis)
    route = []
    for low in range(count):
        high = low | 1 << apart
        if high != low and high < count:
            route += [(low, high), (high, low)]
    return lax.ppermute(block, axis, route)


def handed_down(array, axis, layer):
    return lax.ppermute(array, axis, [(layer, layer + 1)])


def mixed_dot_kernel(sign_ref, values_ref, partner_ref, op_ref, out_ref):
    first = values_ref[...].astype(jnp.float32)
    second = partner_ref[...].astype(jnp.float32)
    mixed = ((second + sign_ref[...] * first) * half_root).astype(jnp.bfloat16)
    width = op_ref.shape[1]
    for start in range(0, width, TILE):
        out_ref[:, start:start + TILE] = jnp.dot(
            mixed, op_ref[:, start:start + TILE], preferred_element_type=jnp.float32
        ).astype(out_ref.dtype)


def transposed_dot_kernel(values_ref, op_ref, out_ref):
    values = values_ref[...]
    width = op_ref.shape[0]
    for start in range(0, width, TILE):
        out_ref[:, start:start + TILE] = lax.dot_general(
            values,
            op_ref[start:start + TILE, :],
            (((1,), (1,)), ((), ())),
            preferred_element_type=jnp.float32,
        ).astype(out_ref.dtype)


def vmem_spec():
    return pl.BlockSpec(memory_space=pltpu.VMEM)


def cost(rows, width):
    return pl.CostEstimate(
        flops=2 * rows * width * width,
        bytes_accessed=2 * width * width + 6 * rows * width,
        transcendentals=0,
    )


def mixed_dot(sign, values, partner, merge_op):
    rows, width = values.shape
    return pl.pallas_call(
        mixed_dot_kernel,
        out_shape=jax.ShapeDtypeStruct(values.shape, jnp.bfloat16),
        in_specs=[vmem_spec()] * 4,
        out_specs=vmem_spec(),
        cost_estimate=cost(rows, width),
        compiler_params=pltpu.CompilerParams(vmem_limit_bytes=4 * 1024 * 1024),
    )(sign, values, partner, pltpu.with_memory_space_constraint(merge_op, pltpu.VMEM))


def transposed_dot(values, merge_op):
    rows, width = values.shape
    return pl.pallas_call(
        transposed_dot_kernel,
        out_shape=jax.ShapeDtypeStruct(values.shape, jnp.bfloat16),
        in_specs=[vmem_spec()] * 2,
        out_specs=vmem_spec(),
        cost_estimate=cost(rows, width),
        compiler_params=pltpu.CompilerParams(vmem_limit_bytes=4 * 1024 * 1024),
    )(values, pltpu.with_memory_space_constraint(merge_op, pltpu.VMEM))


CHUNK = 256


def fetched_dot_kernel(values_in_hbm, sign_ref, values_ref, partner_ref, op_hbm_ref, out_ref, op_ref, own_ref, sems):
    width = op_ref.shape[0]
    blocks = width // CHUNK
    if values_in_hbm:
        own_copy = pltpu.make_async_copy(values_ref, own_ref, sems.at[blocks])
        own_copy.start()
    copies = []
    for index in range(blocks):
        rows = pl.ds(index * CHUNK, CHUNK)
        copy = pltpu.make_async_copy(op_hbm_ref.at[rows, :], op_ref.at[rows, :], sems.at[index])
        copy.start()
        copies.append(copy)
    if values_in_hbm:
        own_copy.wait()
        first = own_ref[...].astype(jnp.float32)
    else:
        first = values_ref[...].astype(jnp.float32)
    second = partner_ref[...].astype(jnp.float32)
    mixed = ((second + sign_ref[...] * first) * half_root).astype(jnp.bfloat16)
    total = jnp.zeros(out_ref.shape, jnp.float32)
    for index, copy in enumerate(copies):
        copy.wait()
        rows = slice(index * CHUNK, (index + 1) * CHUNK)
        total = total + jnp.dot(mixed[:, rows], op_ref[rows, :], preferred_element_type=jnp.float32)
    out_ref[...] = total.astype(out_ref.dtype)


def fetched_dot(sign, values, partner, merge_op, values_in_hbm):
    rows, width = values.shape
    if values_in_hbm:
        values_spec = pl.BlockSpec(memory_space=pl.ANY)
        values = pltpu.with_memory_space_constraint(values, pltpu.HBM)
    else:
        values_spec = vmem_spec()
    return pl.pallas_call(
        functools.partial(fetched_dot_kernel, values_in_hbm),
        out_shape=jax.ShapeDtypeStruct(values.shape, jnp.bfloat16),
        in_specs=[vmem_spec(), values_spec, vmem_spec(), pl.BlockSpec(memory_space=pl.ANY)],
        out_specs=vmem_spec(),
        scratch_shapes=[
            pltpu.VMEM(merge_op.shape, merge_op.dtype),
            pltpu.VMEM(values.shape, values.dtype),
            pltpu.SemaphoreType.DMA((width // CHUNK + 1,)),
        ],
        cost_estimate=cost(rows, width),
        compiler_params=pltpu.CompilerParams(vmem_limit_bytes=16 * 1024 * 1024),
    )(sign, values, partner, pltpu.with_memory_space_constraint(merge_op, pltpu.HBM))

def haar_pair(values, partner, lat_index, bit_level):
    is_lower = lat_index // 2**bit_level % 2 == 0
    first = values.astype(jnp.float32)
    second = partner.astype(jnp.float32)
    return jnp.where(is_lower, (first + second) * half_root, (second - first) * half_root).astype(
        jnp.bfloat16
    )


def level_sign(lat_index, bit_level, width):
    is_lower = lat_index // 2**bit_level % 2 == 0
    return jnp.full((1, width), jnp.where(is_lower, 1.0, -1.0), jnp.float32)


def sweep_layer(leaf_data, merge_op, fetch):
    lat_count = lax.axis_size("lat")
    lat_index = lax.axis_index("lat")
    levels = lat_count.bit_length() - 1
    width = leaf_data.shape[1]
    values = leaf_data
    for bit_level in range(levels):
        partner = partner_2(values, "lat", bit_level)
        sign = level_sign(lat_index, bit_level, width)
        if fetch and bit_level < levels - 1:
            values = fetched_dot(sign, values, partner, merge_op, bit_level == 0)
        else:
            values = mixed_dot(sign, values, partner, merge_op)
    values = transposed_dot(values, merge_op)
    for bit_level in range(levels - 1, -1, -1):
        partner = partner_2(values, "lat", bit_level)
        values = haar_pair(values, partner, lat_index, bit_level)
    return values


def on_device(sources, coupling, merge_ops):
    merge_op = merge_ops[0, 0]
    coupling_row = coupling[0, 0]
    depth_index = lax.axis_index("depth")
    depth_count = lax.axis_size("depth")
    shot_rows = sources[0, 0]
    result = jnp.zeros_like(shot_rows)
    for sweep_step in range(depth_count):
        if sweep_step == 0:
            leaf_data = shot_rows
        else:
            leaf_data = (
                shot_rows.astype(jnp.float32) + coupling_row * incoming.astype(jnp.float32)
            ).astype(jnp.bfloat16)
        solved = sweep_layer(leaf_data, merge_op, sweep_step == 0)
        result = jnp.where(depth_index == sweep_step, solved, result)
        if sweep_step + 1 < depth_count:
            incoming = handed_down(solved, "depth", sweep_step)
    return result[None, None]


def solution(mesh):
    return jax.shard_map(
        on_device,
        mesh=mesh,
        in_specs=(
            P("depth", "lat", None, None),
            P("depth", "lat", None),
            P("depth", "lat", None, None),
        ),
        out_specs=P("depth", "lat", None, None),
        check_vma=False,
    )
```

```python
import functools

import jax
import jax.numpy as jnp
from jax import lax
from jax.experimental import pallas as pl
from jax.experimental.pallas import tpu as pltpu
from jax.sharding import PartitionSpec as P

half_root = 0.7071067811865476
TILE = 512


def partner_2(block, axis, apart):
    count = lax.axis_size(axis)
    route = []
    for low in range(count):
        high = low | 1 << apart
        if high != low and high < count:
            route += [(low, high), (high, low)]
    return lax.ppermute(block, axis, route)


def handed_down(array, axis, layer):
    return lax.ppermute(array, axis, [(layer, layer + 1)])


def mixed_dot_kernel(sign_ref, values_ref, partner_ref, op_ref, out_ref):
    first = values_ref[...].astype(jnp.float32)
    second = partner_ref[...].astype(jnp.float32)
    mixed = ((second + sign_ref[...] * first) * half_root).astype(jnp.bfloat16)
    width = op_ref.shape[1]
    for start in range(0, width, TILE):
        out_ref[:, start:start + TILE] = jnp.dot(
            mixed, op_ref[:, start:start + TILE], preferred_element_type=jnp.float32
        ).astype(out_ref.dtype)


def transposed_dot_kernel(values_ref, op_ref, out_ref):
    values = values_ref[...]
    width = op_ref.shape[0]
    for start in range(0, width, TILE):
        block = lax.dot_general(
            op_ref[start:start + TILE, :],
            values,
            (((1,), (1,)), ((), ())),
            preferred_element_type=jnp.float32,
        )
        out_ref[:, start:start + TILE] = block.T.astype(out_ref.dtype)


def vmem_spec():
    return pl.BlockSpec(memory_space=pltpu.VMEM)


def cost(rows, width):
    return pl.CostEstimate(
        flops=2 * rows * width * width,
        bytes_accessed=2 * width * width + 6 * rows * width,
        transcendentals=0,
    )


def mixed_dot(sign, values, partner, merge_op):
    rows, width = values.shape
    return pl.pallas_call(
        mixed_dot_kernel,
        out_shape=jax.ShapeDtypeStruct(values.shape, jnp.bfloat16),
        in_specs=[vmem_spec()] * 4,
        out_specs=vmem_spec(),
        cost_estimate=cost(rows, width),
        compiler_params=pltpu.CompilerParams(vmem_limit_bytes=4 * 1024 * 1024),
    )(sign, values, partner, pltpu.with_memory_space_constraint(merge_op, pltpu.VMEM))


def transposed_dot(values, merge_op):
    rows, width = values.shape
    return pl.pallas_call(
        transposed_dot_kernel,
        out_shape=jax.ShapeDtypeStruct(values.shape, jnp.bfloat16),
        in_specs=[vmem_spec()] * 2,
        out_specs=vmem_spec(),
        cost_estimate=cost(rows, width),
        compiler_params=pltpu.CompilerParams(vmem_limit_bytes=4 * 1024 * 1024),
    )(values, pltpu.with_memory_space_constraint(merge_op, pltpu.VMEM))


CHUNK = 256


def fetched_dot_kernel(values_in_hbm, sign_ref, values_ref, partner_ref, op_hbm_ref, out_ref, op_ref, own_ref, sems):
    width = op_ref.shape[0]
    blocks = width // CHUNK
    if values_in_hbm:
        own_copy = pltpu.make_async_copy(values_ref, own_ref, sems.at[blocks])
        own_copy.start()
    copies = []
    for index in range(blocks):
        rows = pl.ds(index * CHUNK, CHUNK)
        copy = pltpu.make_async_copy(op_hbm_ref.at[rows, :], op_ref.at[rows, :], sems.at[index])
        copy.start()
        copies.append(copy)
    if values_in_hbm:
        own_copy.wait()
        first = own_ref[...].astype(jnp.float32)
    else:
        first = values_ref[...].astype(jnp.float32)
    second = partner_ref[...].astype(jnp.float32)
    mixed = ((second + sign_ref[...] * first) * half_root).astype(jnp.bfloat16)
    total = jnp.zeros(out_ref.shape, jnp.float32)
    for index, copy in enumerate(copies):
        copy.wait()
        rows = slice(index * CHUNK, (index + 1) * CHUNK)
        total = total + jnp.dot(mixed[:, rows], op_ref[rows, :], preferred_element_type=jnp.float32)
    out_ref[...] = total.astype(out_ref.dtype)


def fetched_dot(sign, values, partner, merge_op, values_in_hbm):
    rows, width = values.shape
    if values_in_hbm:
        values_spec = pl.BlockSpec(memory_space=pl.ANY)
        values = pltpu.with_memory_space_constraint(values, pltpu.HBM)
    else:
        values_spec = vmem_spec()
    return pl.pallas_call(
        functools.partial(fetched_dot_kernel, values_in_hbm),
        out_shape=jax.ShapeDtypeStruct(values.shape, jnp.bfloat16),
        in_specs=[vmem_spec(), values_spec, vmem_spec(), pl.BlockSpec(memory_space=pl.ANY)],
        out_specs=vmem_spec(),
        scratch_shapes=[
            pltpu.VMEM(merge_op.shape, merge_op.dtype),
            pltpu.VMEM(values.shape, values.dtype),
            pltpu.SemaphoreType.DMA((width // CHUNK + 1,)),
        ],
        cost_estimate=cost(rows, width),
        compiler_params=pltpu.CompilerParams(vmem_limit_bytes=16 * 1024 * 1024),
    )(sign, values, partner, pltpu.with_memory_space_constraint(merge_op, pltpu.HBM))

def haar_pair(values, partner, lat_index, bit_level):
    is_lower = lat_index // 2**bit_level % 2 == 0
    first = values.astype(jnp.float32)
    second = partner.astype(jnp.float32)
    return jnp.where(is_lower, (first + second) * half_root, (second - first) * half_root).astype(
        jnp.bfloat16
    )


def level_sign(lat_index, bit_level, width):
    is_lower = lat_index // 2**bit_level % 2 == 0
    return jnp.full((1, width), jnp.where(is_lower, 1.0, -1.0), jnp.float32)


def sweep_layer(leaf_data, merge_op, fetch):
    lat_count = lax.axis_size("lat")
    lat_index = lax.axis_index("lat")
    levels = lat_count.bit_length() - 1
    width = leaf_data.shape[1]
    values = leaf_data
    for bit_level in range(levels):
        partner = partner_2(values, "lat", bit_level)
        sign = level_sign(lat_index, bit_level, width)
        if fetch and bit_level < levels - 1:
            values = fetched_dot(sign, values, partner, merge_op, bit_level == 0)
        else:
            values = mixed_dot(sign, values, partner, merge_op)
    values = transposed_dot(values, merge_op)
    for bit_level in range(levels - 1, -1, -1):
        partner = partner_2(values, "lat", bit_level)
        values = haar_pair(values, partner, lat_index, bit_level)
    return values


def on_device(sources, coupling, merge_ops):
    merge_op = merge_ops[0, 0]
    coupling_row = coupling[0, 0]
    depth_index = lax.axis_index("depth")
    depth_count = lax.axis_size("depth")
    shot_rows = sources[0, 0]
    result = jnp.zeros_like(shot_rows)
    for sweep_step in range(depth_count):
        if sweep_step == 0:
            leaf_data = shot_rows
        else:
            leaf_data = (
                shot_rows.astype(jnp.float32) + coupling_row * incoming.astype(jnp.float32)
            ).astype(jnp.bfloat16)
        solved = sweep_layer(leaf_data, merge_op, sweep_step == 0)
        result = jnp.where(depth_index == sweep_step, solved, result)
        if sweep_step + 1 < depth_count:
            incoming = handed_down(solved, "depth", sweep_step)
    return result[None, None]


def solution(mesh):
    return jax.shard_map(
        on_device,
        mesh=mesh,
        in_specs=(
            P("depth", "lat", None, None),
            P("depth", "lat", None),
            P("depth", "lat", None, None),
        ),
        out_specs=P("depth", "lat", None, None),
        check_vma=False,
    )
```

```python
import functools

import jax
import jax.numpy as jnp
from jax import lax
from jax.experimental import pallas as pl
from jax.experimental.pallas import tpu as pltpu
from jax.sharding import PartitionSpec as P


half_root = 0.7071067811865476
TILE = 512


def partner_2(block, axis, apart):
    count = lax.axis_size(axis)
    route = []
    for low in range(count):
        high = low | 1 << apart
        if high != low and high < count:
            route += [(low, high), (high, low)]
    return lax.ppermute(block, axis, route)


def handed_down(array, axis, layer):
    return lax.ppermute(array, axis, [(layer, layer + 1)])


def mixed_dot_kernel(sign_ref, values_ref, partner_ref, op_ref, out_ref):
    first = values_ref[...].astype(jnp.float32)
    second = partner_ref[...].astype(jnp.float32)
    mixed = ((second + sign_ref[...] * first) * half_root).astype(jnp.bfloat16)
    width = op_ref.shape[1]
    for start in range(0, width, TILE):
        out_ref[:, start:start + TILE] = jnp.dot(
            mixed, op_ref[:, start:start + TILE], preferred_element_type=jnp.float32
        ).astype(out_ref.dtype)


def transposed_dot_kernel(values_ref, op_ref, out_ref):
    values = values_ref[...]
    width = op_ref.shape[0]
    for start in range(0, width, TILE):
        block = lax.dot_general(
            op_ref[start:start + TILE, :],
            values,
            (((1,), (1,)), ((), ())),
            preferred_element_type=jnp.float32,
        )
        out_ref[:, start:start + TILE] = block.T.astype(out_ref.dtype)


def vmem_spec():
    return pl.BlockSpec(memory_space=pltpu.VMEM)


def cost(rows, width):
    return pl.CostEstimate(
        flops=2 * rows * width * width,
        bytes_accessed=2 * width * width + 6 * rows * width,
        transcendentals=0,
    )


def mixed_dot(sign, values, partner, merge_op):
    rows, width = values.shape
    return pl.pallas_call(
        mixed_dot_kernel,
        out_shape=jax.ShapeDtypeStruct(values.shape, jnp.bfloat16),
        in_specs=[vmem_spec()] * 4,
        out_specs=vmem_spec(),
        cost_estimate=cost(rows, width),
        compiler_params=pltpu.CompilerParams(vmem_limit_bytes=4 * 1024 * 1024),
    )(sign, values, partner, pltpu.with_memory_space_constraint(merge_op, pltpu.VMEM))


def transposed_dot(values, merge_op):
    rows, width = values.shape
    return pl.pallas_call(
        transposed_dot_kernel,
        out_shape=jax.ShapeDtypeStruct(values.shape, jnp.bfloat16),
        in_specs=[vmem_spec()] * 2,
        out_specs=vmem_spec(),
        cost_estimate=cost(rows, width),
        compiler_params=pltpu.CompilerParams(vmem_limit_bytes=4 * 1024 * 1024),
    )(values, pltpu.with_memory_space_constraint(merge_op, pltpu.VMEM))


CHUNK = 256


def fetched_dot_kernel(values_in_hbm, sign_ref, values_ref, partner_ref, op_hbm_ref, out_ref, op_ref, own_ref, sems):
    width = op_ref.shape[0]
    blocks = width // CHUNK
    if values_in_hbm:
        own_copy = pltpu.make_async_copy(values_ref, own_ref, sems.at[blocks])
        own_copy.start()
    copies = []
    for index in range(blocks):
        rows = pl.ds(index * CHUNK, CHUNK)
        copy = pltpu.make_async_copy(op_hbm_ref.at[rows, :], op_ref.at[rows, :], sems.at[index])
        copy.start()
        copies.append(copy)
    if values_in_hbm:
        own_copy.wait()
        first = own_ref[...].astype(jnp.float32)
    else:
        first = values_ref[...].astype(jnp.float32)
    second = partner_ref[...].astype(jnp.float32)
    mixed = ((second + sign_ref[...] * first) * half_root).astype(jnp.bfloat16)
    total = jnp.zeros(out_ref.shape, jnp.float32)
    for index, copy in enumerate(copies):
        copy.wait()
        rows = slice(index * CHUNK, (index + 1) * CHUNK)
        total = total + jnp.dot(mixed[:, rows], op_ref[rows, :], preferred_element_type=jnp.float32)
    out_ref[...] = total.astype(out_ref.dtype)


def fetched_dot(sign, values, partner, merge_op, values_in_hbm):
    rows, width = values.shape
    if values_in_hbm:
        values_spec = pl.BlockSpec(memory_space=pl.ANY)
        values = pltpu.with_memory_space_constraint(values, pltpu.HBM)
    else:
        values_spec = vmem_spec()
    return pl.pallas_call(
        functools.partial(fetched_dot_kernel, values_in_hbm),
        out_shape=jax.ShapeDtypeStruct(values.shape, jnp.bfloat16),
        in_specs=[vmem_spec(), values_spec, vmem_spec(), pl.BlockSpec(memory_space=pl.ANY)],
        out_specs=vmem_spec(),
        scratch_shapes=[
            pltpu.VMEM(merge_op.shape, merge_op.dtype),
            pltpu.VMEM(values.shape, values.dtype),
            pltpu.SemaphoreType.DMA((width // CHUNK + 1,)),
        ],
        cost_estimate=cost(rows, width),
        compiler_params=pltpu.CompilerParams(vmem_limit_bytes=16 * 1024 * 1024),
    )(sign, values, partner, pltpu.with_memory_space_constraint(merge_op, pltpu.HBM))


def warm_kernel(values_ref, op_ref, out_ref):
    out_ref[...] = values_ref[0:8, 0:128].astype(jnp.float32) * 0.0


def warmed(values, merge_op):
    return pl.pallas_call(
        warm_kernel,
        out_shape=jax.ShapeDtypeStruct((8, 128), jnp.float32),
        in_specs=[vmem_spec()] * 2,
        out_specs=vmem_spec(),
        compiler_params=pltpu.CompilerParams(vmem_limit_bytes=4 * 1024 * 1024, has_side_effects=True),
    )(values, pltpu.with_memory_space_constraint(merge_op, pltpu.VMEM))


def haar_pair(values, partner, lat_index, bit_level):
    is_lower = lat_index // 2**bit_level % 2 == 0
    first = values.astype(jnp.float32)
    second = partner.astype(jnp.float32)
    return jnp.where(is_lower, (first + second) * half_root, (second - first) * half_root).astype(
        jnp.bfloat16
    )


def level_sign(lat_index, bit_level, width):
    is_lower = lat_index // 2**bit_level % 2 == 0
    return jnp.full((1, width), jnp.where(is_lower, 1.0, -1.0), jnp.float32)


def sweep_layer(leaf_data, merge_op, fetch):
    lat_count = lax.axis_size("lat")
    lat_index = lax.axis_index("lat")
    levels = lat_count.bit_length() - 1
    width = leaf_data.shape[1]
    values = leaf_data
    for bit_level in range(levels):
        if fetch and bit_level > 0:
            partner = partner_2(values, "lat", bit_level)
            warmed(values, merge_op)
        else:
            partner = partner_2(values, "lat", bit_level)
        sign = level_sign(lat_index, bit_level, width)
        if fetch and bit_level == 0:
            values = fetched_dot(sign, values, partner, merge_op, bit_level == 0)
        else:
            values = mixed_dot(sign, values, partner, merge_op)
    values = transposed_dot(values, merge_op)
    for bit_level in range(levels - 1, -1, -1):
        partner = partner_2(values, "lat", bit_level)
        values = haar_pair(values, partner, lat_index, bit_level)
    return values


def on_device(sources, coupling, merge_ops):
    merge_op = merge_ops[0, 0]
    coupling_row = coupling[0, 0]
    depth_index = lax.axis_index("depth")
    depth_count = lax.axis_size("depth")
    shot_rows = sources[0, 0]
    result = jnp.zeros_like(shot_rows)
    for sweep_step in range(depth_count):
        if sweep_step == 0:
            leaf_data = shot_rows
        else:
            leaf_data = (
                shot_rows.astype(jnp.float32) + coupling_row * incoming.astype(jnp.float32)
            ).astype(jnp.bfloat16)
        if sweep_step == 0:
            solved = sweep_layer(leaf_data, merge_op, True)
        else:
            solved = sweep_layer(leaf_data, merge_op, False)
        result = jnp.where(depth_index == sweep_step, solved, result)
        if sweep_step + 1 < depth_count:
            incoming = handed_down(solved, "depth", sweep_step)
    return result[None, None]


def solution(mesh):
    return jax.shard_map(
        on_device,
        mesh=mesh,
        in_specs=(
            P("depth", "lat", None, None),
            P("depth", "lat", None),
            P("depth", "lat", None, None),
        ),
        out_specs=P("depth", "lat", None, None),
        check_vma=False,
    )
```

```python
import functools

import jax
import jax.numpy as jnp
from jax import lax
from jax.experimental import pallas as pl
from jax.experimental.pallas import tpu as pltpu
from jax.sharding import PartitionSpec as P


half_root = 0.7071067811865476
TILE = 512


def partner_2(block, axis, apart):
    count = lax.axis_size(axis)
    route = []
    for low in range(count):
        high = low | 1 << apart
        if high != low and high < count:
            route += [(low, high), (high, low)]
    return lax.ppermute(block, axis, route)


def handed_down(array, axis, layer):
    return lax.ppermute(array, axis, [(layer, layer + 1)])


def mixed_dot_kernel(sign_ref, values_ref, partner_ref, op_ref, out_ref):
    first = values_ref[...].astype(jnp.float32)
    second = partner_ref[...].astype(jnp.float32)
    mixed = ((second + sign_ref[...] * first) * half_root).astype(jnp.bfloat16)
    width = op_ref.shape[1]
    for start in range(0, width, TILE):
        out_ref[:, start:start + TILE] = jnp.dot(
            mixed, op_ref[:, start:start + TILE], preferred_element_type=jnp.float32
        ).astype(out_ref.dtype)


def transposed_dot_kernel(values_ref, op_ref, out_ref):
    values = values_ref[...]
    width = op_ref.shape[0]
    for start in range(0, width, TILE):
        block = lax.dot_general(
            op_ref[start:start + TILE, :],
            values,
            (((1,), (1,)), ((), ())),
            preferred_element_type=jnp.float32,
        )
        out_ref[:, start:start + TILE] = block.T.astype(out_ref.dtype)


def vmem_spec():
    return pl.BlockSpec(memory_space=pltpu.VMEM)


def cost(rows, width):
    return pl.CostEstimate(
        flops=2 * rows * width * width,
        bytes_accessed=2 * width * width + 6 * rows * width,
        transcendentals=0,
    )


def mixed_dot(sign, values, partner, merge_op):
    rows, width = values.shape
    return pl.pallas_call(
        mixed_dot_kernel,
        out_shape=jax.ShapeDtypeStruct(values.shape, jnp.bfloat16),
        in_specs=[vmem_spec()] * 4,
        out_specs=vmem_spec(),
        cost_estimate=cost(rows, width),
        compiler_params=pltpu.CompilerParams(vmem_limit_bytes=4 * 1024 * 1024),
    )(sign, values, partner, pltpu.with_memory_space_constraint(merge_op, pltpu.VMEM))


def transposed_dot(values, merge_op):
    rows, width = values.shape
    return pl.pallas_call(
        transposed_dot_kernel,
        out_shape=jax.ShapeDtypeStruct(values.shape, jnp.bfloat16),
        in_specs=[vmem_spec()] * 2,
        out_specs=vmem_spec(),
        cost_estimate=cost(rows, width),
        compiler_params=pltpu.CompilerParams(vmem_limit_bytes=4 * 1024 * 1024),
    )(values, pltpu.with_memory_space_constraint(merge_op, pltpu.VMEM))


CHUNK = 128


def fetched_dot_kernel(values_in_hbm, sign_ref, values_ref, partner_ref, op_hbm_ref, out_ref, op_ref, own_ref, sems):
    width = op_ref.shape[0]
    blocks = width // CHUNK
    if values_in_hbm:
        own_copy = pltpu.make_async_copy(values_ref, own_ref, sems.at[blocks])
        own_copy.start()
    copies = []
    for index in range(blocks):
        rows = pl.ds(index * CHUNK, CHUNK)
        copy = pltpu.make_async_copy(op_hbm_ref.at[rows, :], op_ref.at[rows, :], sems.at[index])
        copy.start()
        copies.append(copy)
    if values_in_hbm:
        own_copy.wait()
        first = own_ref[...].astype(jnp.float32)
    else:
        first = values_ref[...].astype(jnp.float32)
    second = partner_ref[...].astype(jnp.float32)
    mixed = ((second + sign_ref[...] * first) * half_root).astype(jnp.bfloat16)
    total = jnp.zeros(out_ref.shape, jnp.float32)
    for index, copy in enumerate(copies):
        copy.wait()
        rows = slice(index * CHUNK, (index + 1) * CHUNK)
        total = total + jnp.dot(mixed[:, rows], op_ref[rows, :], preferred_element_type=jnp.float32)
    out_ref[...] = total.astype(out_ref.dtype)


def fetched_dot(sign, values, partner, merge_op, values_in_hbm):
    rows, width = values.shape
    if values_in_hbm:
        values_spec = pl.BlockSpec(memory_space=pl.ANY)
        values = pltpu.with_memory_space_constraint(values, pltpu.HBM)
    else:
        values_spec = vmem_spec()
    return pl.pallas_call(
        functools.partial(fetched_dot_kernel, values_in_hbm),
        out_shape=jax.ShapeDtypeStruct(values.shape, jnp.bfloat16),
        in_specs=[vmem_spec(), values_spec, vmem_spec(), pl.BlockSpec(memory_space=pl.ANY)],
        out_specs=vmem_spec(),
        scratch_shapes=[
            pltpu.VMEM(merge_op.shape, merge_op.dtype),
            pltpu.VMEM(values.shape, values.dtype),
            pltpu.SemaphoreType.DMA((width // CHUNK + 1,)),
        ],
        cost_estimate=cost(rows, width),
        compiler_params=pltpu.CompilerParams(vmem_limit_bytes=16 * 1024 * 1024),
    )(sign, values, partner, pltpu.with_memory_space_constraint(merge_op, pltpu.HBM))


def warm_kernel(values_ref, op_ref, out_ref):
    out_ref[...] = values_ref[0:8, 0:128].astype(jnp.float32) * 0.0


def warmed(values, merge_op):
    return pl.pallas_call(
        warm_kernel,
        out_shape=jax.ShapeDtypeStruct((8, 128), jnp.float32),
        in_specs=[vmem_spec()] * 2,
        out_specs=vmem_spec(),
        compiler_params=pltpu.CompilerParams(vmem_limit_bytes=4 * 1024 * 1024, has_side_effects=True),
    )(values, pltpu.with_memory_space_constraint(merge_op, pltpu.VMEM))


def haar_pair(values, partner, lat_index, bit_level):
    is_lower = lat_index // 2**bit_level % 2 == 0
    first = values.astype(jnp.float32)
    second = partner.astype(jnp.float32)
    return jnp.where(is_lower, (first + second) * half_root, (second - first) * half_root).astype(
        jnp.bfloat16
    )


def level_sign(lat_index, bit_level, width):
    is_lower = lat_index // 2**bit_level % 2 == 0
    return jnp.full((1, width), jnp.where(is_lower, 1.0, -1.0), jnp.float32)


def sweep_layer(leaf_data, merge_op, fetch):
    lat_count = lax.axis_size("lat")
    lat_index = lax.axis_index("lat")
    levels = lat_count.bit_length() - 1
    width = leaf_data.shape[1]
    values = leaf_data
    for bit_level in range(levels):
        if fetch and bit_level == levels - 1:
            partner = partner_2(values, "lat", bit_level)
            warmed(values, merge_op)
        else:
            partner = partner_2(values, "lat", bit_level)
        sign = level_sign(lat_index, bit_level, width)
        if fetch and bit_level < levels - 1:
            values = fetched_dot(sign, values, partner, merge_op, bit_level == 0)
        else:
            values = mixed_dot(sign, values, partner, merge_op)
    values = transposed_dot(values, merge_op)
    for bit_level in range(levels - 1, -1, -1):
        partner = partner_2(values, "lat", bit_level)
        values = haar_pair(values, partner, lat_index, bit_level)
    return values


def on_device(sources, coupling, merge_ops):
    merge_op = merge_ops[0, 0]
    coupling_row = coupling[0, 0]
    depth_index = lax.axis_index("depth")
    depth_count = lax.axis_size("depth")
    shot_rows = sources[0, 0]
    result = jnp.zeros_like(shot_rows)
    for sweep_step in range(depth_count):
        if sweep_step == 0:
            leaf_data = shot_rows
        else:
            leaf_data = (
                shot_rows.astype(jnp.float32) + coupling_row * incoming.astype(jnp.float32)
            ).astype(jnp.bfloat16)
        if sweep_step == 0:
            solved = sweep_layer(leaf_data, merge_op, True)
        else:
            solved = sweep_layer(leaf_data, merge_op, False)
        result = jnp.where(depth_index == sweep_step, solved, result)
        if sweep_step + 1 < depth_count:
            incoming = handed_down(solved, "depth", sweep_step)
    return result[None, None]


def solution(mesh):
    return jax.shard_map(
        on_device,
        mesh=mesh,
        in_specs=(
            P("depth", "lat", None, None),
            P("depth", "lat", None),
            P("depth", "lat", None, None),
        ),
        out_specs=P("depth", "lat", None, None),
        check_vma=False,
    )
```
